32 devices in a mesh: freq: 4 (over y, core), row: 8 (over z, x).
Axes of the slice: x: 2, y: 2, z: 4, core: 2. Of those that a mesh axis runs over, the one named last changes fastest.
Arguments:
- traces: bfloat16 [2, 8192, 8192], P(None, ('freq', 'row')), may hold values from -1.1953125 to 1.1953125
- prior: bfloat16 [4, 2, 8192, 8192], P('freq', None, None, 'row'), may hold values from -0.796875 to 0.796875
- bins: int32 [4], replicated, may hold values from 64 to 255
- panels: int32 [2], replicated, may hold values from 0 to 31
Outputs:
- multiples: bfloat16 [4, 2, 8192, 8192], P('freq', None, 'row')
- spectrum: bfloat16 [4, 2, 8192, 8192], P('freq', None, None, 'row')
The draws below stay inside these ranges and needn't reach their ends.
All inputs are finite; a program needn't handle non-finite values.
Results may differ from the reference program's by a relative error of at most 0.0077.
Values may be sent and summed in bfloat16 or wider, within the bound.
No kernel may reach another device: no remote copies, remote signals or barrier semaphores. Data moves between devices by JAX's collectives and lax.ppermute only.
A program may use at most 640 MiB of HBM per device.

```python
import math
import jax
import jax.numpy as jnp
from jax import lax

STATIONS = 8192
NT_REC = 1024
NT_BLK = 2
PANEL = 256
STEPS = 2
NF = 4
BLOCK_START = 1022


def plant(drawn, stream_key, least, largest):
    shape = drawn.shape
    index_at = [jax.random.randint(jax.random.fold_in(stream_key, axis), (), 0, shape[axis]) for axis in range(len(shape))]
    drawn = drawn.at[tuple(index_at)].set(least)
    longest = shape.index(max(shape))
    index_at[longest] = (index_at[longest] + 1) % shape[longest]
    return drawn.at[tuple(index_at)].set(largest)


def block_levels(stream_key, shape, cuts, low, high):
    loudness, own = 1.0, jax.random.fold_in(stream_key, 6)
    for axis_at, shards_of in cuts:
        steps = jnp.exp(jax.random.uniform(jax.random.fold_in(own, axis_at), (shards_of,), jnp.float32, low / len(cuts), high / len(cuts)))
        loudness = loudness * jnp.repeat(steps, shape[axis_at] // shards_of).reshape([-1 if axis == axis_at else 1 for axis in range(len(shape))])
    return loudness


def scatter_about(key, extent, spread, most, shards=(), kind=jnp.bfloat16):
    values = jax.random.normal(key, extent, jnp.float32) * spread
    if len(shards) > 0:
        values = block_levels(key, extent, shards, -0.22, 0.18) * values
    return jnp.clip(values, min=-most, max=most).astype(kind)


def setup_inputs(seed: int = 0) -> dict:
    arg_keys = jax.random.split(jax.random.key(seed), 5)
    traces = scatter_about(arg_keys[0], (NT_BLK, STATIONS, STATIONS), 0.15, 1.1953125, ((1, 32),))
    prior = scatter_about(arg_keys[1], (NF, 2, STATIONS, STATIONS), 0.1, 0.796875, ((0, 4), (3, 8)))
    bins = plant(jax.random.randint(arg_keys[2], (NF,), NT_REC // 16, NT_REC // 4), jax.random.fold_in(arg_keys[2], 1), NT_REC // 16, (NT_REC // 4) - 1).astype(jnp.int32)
    panels = jax.random.randint(arg_keys[3], (STEPS,), 0, STATIONS // PANEL).astype(jnp.int32)
    return dict(traces=traces, prior=prior, bins=bins, panels=panels)


def complex_terms(left, right):
    dims = (((0,), (1,)), ((), ()))

    def product(first, second):
        return lax.dot_general(first, second, dims, preferred_element_type=jnp.float32)

    real_part = product(left[0], right[0]) - product(left[1], right[1])
    imag_part = product(left[0], right[1]) + product(left[1], right[0])
    return real_part, imag_part


def reference(traces, prior, bins, panels):
    sample_index = BLOCK_START + jnp.arange(NT_BLK, dtype=jnp.int32)
    turn_count = (bins.astype(jnp.int32)[:, None] * sample_index[None, :]) % NT_REC
    angles = (2.0 * math.pi / NT_REC) * turn_count.astype(jnp.float32)
    twiddle = jnp.stack([jnp.cos(angles), -jnp.sin(angles)], axis=1).astype(jnp.bfloat16)
    samples = traces.astype(jnp.float32)
    results = []
    spectra = []
    for frequency in range(NF):
        transformed = jnp.einsum("tsr,ct->csr", samples, twiddle[frequency].astype(jnp.float32)).astype(jnp.bfloat16)
        spectrum = (prior[frequency].astype(jnp.float32) + transformed.astype(jnp.float32)).astype(jnp.bfloat16)
        spectra.append(spectrum)
        real_sum = jnp.zeros((STATIONS, STATIONS), jnp.float32)
        imag_sum = jnp.zeros((STATIONS, STATIONS), jnp.float32)
        for panel_step in range(STEPS):
            first_row = (panels[panel_step] * PANEL).astype(jnp.int32)
            left = lax.dynamic_slice_in_dim(spectrum, first_row, PANEL, 1)
            right = lax.dynamic_slice_in_dim(spectrum, first_row, PANEL, 2)
            real_part, imag_part = complex_terms(left, right)
            real_sum = real_sum + real_part
            imag_sum = imag_sum + imag_part
        results.append(jnp.stack([real_sum, imag_sum]).astype(jnp.bfloat16))
    return (jnp.stack(results), jnp.stack(spectra))
```

```python
import math

import jax
import jax.numpy as jnp
from jax import lax
from jax.sharding import PartitionSpec as P

NT_REC = 1024
PANEL = 256
STEPS = 2
BLOCK_START = 1022


def spread(value, axis, source):
    kept = jnp.where(lax.axis_index(axis) == source, value, 0).astype(value.dtype)
    return lax.psum(kept, axis)


def complex_terms(left, right):
    dims = (((0,), (1,)), ((), ()))

    def product(first, second):
        return lax.dot_general(first, second, dims, preferred_element_type=jnp.float32)

    real_part = product(left[0], right[0]) - product(left[1], right[1])
    imag_part = product(left[0], right[1]) + product(left[1], right[0])
    return (real_part, imag_part)


def body(traces, prior, bins, panels):
    sample_count, shots_local, receivers = traces.shape
    row_count = lax.axis_size("row")
    block_rows = receivers // row_count
    sample_index = BLOCK_START + jnp.arange(sample_count, dtype=jnp.int32)
    turn_count = bins[:, None] * sample_index[None, :] % NT_REC
    angles = 2.0 * math.pi / NT_REC * turn_count.astype(jnp.float32)
    twiddle = jnp.stack([jnp.cos(angles), -jnp.sin(angles)], axis=1).astype(jnp.bfloat16)
    own_twiddle = lax.dynamic_index_in_dim(twiddle, lax.axis_index("freq"), 0, keepdims=False)
    by_row = lax.all_to_all(traces, "row", split_axis=2, concat_axis=1, tiled=True)
    gathered = lax.all_gather(by_row, "freq", axis=1, tiled=True)
    transformed = jnp.einsum(
        "tsb,ct->csb", gathered, own_twiddle, preferred_element_type=jnp.float32
    ).astype(jnp.bfloat16)
    spectrum = (prior[0].astype(jnp.float32) + transformed.astype(jnp.float32)).astype(jnp.bfloat16)
    panels_each = block_rows // PANEL
    real_sum = jnp.zeros((block_rows, receivers), jnp.float32)
    imag_sum = jnp.zeros((block_rows, receivers), jnp.float32)
    for panel_step in range(STEPS):
        chosen = panels[panel_step]
        owner = chosen // panels_each
        offset = chosen % panels_each * PANEL
        own_rows = lax.dynamic_slice_in_dim(spectrum, offset, PANEL, 2)
        panel_data = spread(own_rows, "row", owner)
        left = lax.dynamic_slice_in_dim(spectrum, chosen * PANEL, PANEL, 1)
        real_part, imag_part = complex_terms(left, panel_data)
        real_sum = real_sum + real_part
        imag_sum = imag_sum + imag_part
    return (jnp.stack([real_sum, imag_sum])[None].astype(jnp.bfloat16), spectrum[None])


def solution(mesh):
    return jax.shard_map(
        body,
        mesh=mesh,
        in_specs=(P(None, ("freq", "row"), None), P("freq", None, None, "row"), P(), P()),
        out_specs=(P("freq", None, "row", None), P("freq", None, None, "row")),
        check_vma=False,
    )
```

```python
import math

import jax
import jax.numpy as jnp
from jax import lax
from jax.sharding import PartitionSpec as P

NT_REC = 1024
PANEL = 256
STEPS = 2
BLOCK_START = 1022
PIECES = 2


def spread(value, axis, source):
    kept = jnp.where(lax.axis_index(axis) == source, value, 0).astype(value.dtype)
    return lax.psum(kept, axis)


def to_bf16(value):
    return lax.reduce_precision(value, exponent_bits=8, mantissa_bits=7).astype(jnp.bfloat16)


def body(traces, prior, bins, panels):
    sample_count, shots_local, receivers = traces.shape
    row_count = lax.axis_size("row")
    freq_count = lax.axis_size("freq")
    block_rows = receivers // row_count
    sample_index = BLOCK_START + jnp.arange(sample_count, dtype=jnp.int32)
    turn_count = bins[:, None] * sample_index[None, :] % NT_REC
    angles = 2.0 * math.pi / NT_REC * turn_count.astype(jnp.float32)
    twiddle = jnp.stack([jnp.cos(angles), -jnp.sin(angles)], axis=1).astype(jnp.bfloat16)
    own_twiddle = lax.dynamic_index_in_dim(twiddle, lax.axis_index("freq"), 0, keepdims=False)
    weights = own_twiddle.astype(jnp.float32)
    piece = shots_local // PIECES
    groups = freq_count * row_count
    prior_blocks = prior[0].reshape(2, groups, PIECES, piece, block_rows)
    parts = []
    for index in range(PIECES):
        chunk = traces[:, index * piece:(index + 1) * piece, :]
        by_row = lax.all_to_all(chunk, "row", split_axis=2, concat_axis=1, tiled=True)
        gathered = lax.all_gather(by_row, "freq", axis=1, tiled=True).astype(jnp.float32)
        gathered = gathered.reshape(sample_count, groups, piece, block_rows)
        transformed = weights[:, 0, None, None, None] * gathered[0] + weights[:, 1, None, None, None] * gathered[1]
        transformed = lax.reduce_precision(transformed, exponent_bits=8, mantissa_bits=7)
        parts.append(to_bf16(prior_blocks[:, :, index].astype(jnp.float32) + transformed))
    spectrum = jnp.stack(parts, axis=2).reshape(2, receivers, block_rows)
    panels_each = block_rows // PANEL
    lefts = []
    reals = []
    imags = []
    for panel_step in range(STEPS):
        chosen = panels[panel_step]
        owner = chosen // panels_each
        offset = chosen % panels_each * PANEL
        own_rows = lax.dynamic_slice_in_dim(spectrum, offset, PANEL, 2)
        right = spread(own_rows, "row", owner)
        left = lax.dynamic_slice_in_dim(spectrum, chosen * PANEL, PANEL, 1)
        lefts += [left[0], left[1]]
        reals += [right[0], -right[1]]
        imags += [right[1], right[0]]
    left_all = jnp.concatenate(lefts, axis=0)
    dims = (((0,), (1,)), ((), ()))
    real_sum = lax.dot_general(left_all, jnp.concatenate(reals, axis=1), dims, preferred_element_type=jnp.float32)
    imag_sum = lax.dot_general(left_all, jnp.concatenate(imags, axis=1), dims, preferred_element_type=jnp.float32)
    return (jnp.stack([real_sum, imag_sum])[None].astype(jnp.bfloat16), spectrum[None])


def solution(mesh):
    return jax.shard_map(
        body,
        mesh=mesh,
        in_specs=(P(None, ("freq", "row"), None), P("freq", None, None, "row"), P(), P()),
        out_specs=(P("freq", None, "row", None), P("freq", None, None, "row")),
        check_vma=False,
    )
```

```python
import math

import jax
import jax.numpy as jnp
from jax import lax
from jax.sharding import PartitionSpec as P

NT_REC = 1024
PANEL = 256
STEPS = 2
BLOCK_START = 1022
PIECES = 2
RING_CHUNKS = 8


def ring_order(count):
    evens = list(range(0, count, 2))
    odds = list(range(1, count, 2))[::-1]
    return evens + odds


def broadcast(values, owners, chunks):
    count = lax.axis_size("row")
    order = ring_order(count)
    place = [0] * count
    for position, member in enumerate(order):
        place[member] = position
    place_of = jnp.array(place, jnp.int32)
    mine = place_of[lax.axis_index("row")]
    forward = [(order[i], order[(i + 1) % count]) for i in range(count)]
    backward = [(order[(i + 1) % count], order[i]) for i in range(count)]
    steps = chunks + count - 2
    halves = []
    for direction, pairs in ((0, forward), (1, backward)):
        distance = []
        own = []
        for value, owner in zip(values, owners):
            if direction == 0:
                distance.append((mine - place_of[owner]) % count)
            else:
                distance.append((place_of[owner] - mine) % count)
            half = value.shape[1] // 2
            part = value[:, direction * half:(direction + 1) * half]
            own.append(part.reshape(part.shape[0], chunks, half // chunks, *part.shape[2:]))
        held = [jnp.zeros_like(piece[:, 0]) for piece in own]
        arrived = [[] for _ in values]
        for step in range(steps):
            send = [
                jnp.where(distance[p] == 0, own[p][:, min(step, chunks - 1)], held[p])
                for p in range(len(values))
            ]
            held = lax.ppermute(send, "row", pairs)
            for p in range(len(values)):
                arrived[p].append(held[p])
        results = []
        for p in range(len(values)):
            stacked = jnp.stack(arrived[p], axis=1)
            start = jnp.maximum(distance[p] - 1, 0)
            picked = lax.dynamic_slice_in_dim(stacked, start, chunks, 1)
            picked = jnp.where(distance[p] == 0, own[p], picked)
            results.append(picked.reshape(picked.shape[0], -1, *picked.shape[3:]))
        halves.append(results)
    return [jnp.concatenate([halves[0][p], halves[1][p]], axis=1) for p in range(len(values))]


def to_bf16(value):
    return lax.reduce_precision(value, exponent_bits=8, mantissa_bits=7).astype(jnp.bfloat16)


def body(traces, prior, bins, panels):
    sample_count, shots_local, receivers = traces.shape
    row_count = lax.axis_size("row")
    freq_count = lax.axis_size("freq")
    block_rows = receivers // row_count
    sample_index = BLOCK_START + jnp.arange(sample_count, dtype=jnp.int32)
    turn_count = bins[:, None] * sample_index[None, :] % NT_REC
    angles = 2.0 * math.pi / NT_REC * turn_count.astype(jnp.float32)
    twiddle = jnp.stack([jnp.cos(angles), -jnp.sin(angles)], axis=1).astype(jnp.bfloat16)
    own_twiddle = lax.dynamic_index_in_dim(twiddle, lax.axis_index("freq"), 0, keepdims=False)
    weights = own_twiddle.astype(jnp.float32)
    piece = shots_local // PIECES
    groups = freq_count * row_count
    prior_blocks = prior[0].reshape(2, groups, PIECES, piece, block_rows)
    parts = []
    for index in range(PIECES):
        chunk = traces[:, index * piece:(index + 1) * piece, :]
        by_row = lax.all_to_all(chunk, "row", split_axis=2, concat_axis=1, tiled=True)
        gathered = lax.all_gather(by_row, "freq", axis=1, tiled=True).astype(jnp.float32)
        gathered = gathered.reshape(sample_count, groups, piece, block_rows)
        transformed = weights[:, 0, None, None, None] * gathered[0] + weights[:, 1, None, None, None] * gathered[1]
        transformed = lax.reduce_precision(transformed, exponent_bits=8, mantissa_bits=7)
        parts.append(to_bf16(prior_blocks[:, :, index].astype(jnp.float32) + transformed))
    spectrum = jnp.stack(parts, axis=2).reshape(2, receivers, block_rows)
    panels_each = block_rows // PANEL
    own_panels = []
    owners = []
    lefts = []
    for panel_step in range(STEPS):
        chosen = panels[panel_step]
        owners.append(chosen // panels_each)
        offset = chosen % panels_each * PANEL
        own_panels.append(lax.dynamic_slice_in_dim(spectrum, offset, PANEL, 2))
        left = lax.dynamic_slice_in_dim(spectrum, chosen * PANEL, PANEL, 1)
        lefts += [left[0], left[1]]
    rights = broadcast(own_panels, owners, RING_CHUNKS)
    reals = []
    imags = []
    for right in rights:
        reals += [right[0], -right[1]]
        imags += [right[1], right[0]]
    left_all = jnp.concatenate(lefts, axis=0)
    dims = (((0,), (1,)), ((), ()))
    real_sum = lax.dot_general(left_all, jnp.concatenate(reals, axis=1), dims, preferred_element_type=jnp.float32)
    imag_sum = lax.dot_general(left_all, jnp.concatenate(imags, axis=1), dims, preferred_element_type=jnp.float32)
    return (jnp.stack([real_sum, imag_sum])[None].astype(jnp.bfloat16), spectrum[None])


def solution(mesh):
    return jax.shard_map(
        body,
        mesh=mesh,
        in_specs=(P(None, ("freq", "row"), None), P("freq", None, None, "row"), P(), P()),
        out_specs=(P("freq", None, "row", None), P("freq", None, None, "row")),
        check_vma=False,
    )
```

```python
import math

import jax
import jax.numpy as jnp
from jax import lax
from jax.sharding import PartitionSpec as P

NT_REC = 1024
PANEL = 256
STEPS = 2
BLOCK_START = 1022
PIECES = 2
RING_CHUNKS = 16


def ring_order(count):
    evens = list(range(0, count, 2))
    odds = list(range(1, count, 2))[::-1]
    return evens + odds


def broadcast(value, owners, chunks):
    count = lax.axis_size("row")
    order = ring_order(count)
    place = [0] * count
    for position, member in enumerate(order):
        place[member] = position
    place_of = jnp.array(place, jnp.int32)
    mine = place_of[lax.axis_index("row")]
    owner_place = place_of[owners]
    forward = [(order[i], order[(i + 1) % count]) for i in range(count)]
    backward = [(order[(i + 1) % count], order[i]) for i in range(count)]
    steps = chunks + count - 2
    lead = (1,) * (value.ndim - 1)
    halves = []
    for direction, pairs in ((0, forward), (1, backward)):
        if direction == 0:
            distance = (mine - owner_place) % count
        else:
            distance = (owner_place - mine) % count
        half = value.shape[2] // 2
        part = value[:, :, direction * half:(direction + 1) * half]
        own = part.reshape(*part.shape[:2], chunks, half // chunks, *part.shape[3:])
        is_owner = (distance == 0).reshape(-1, *lead)
        held = jnp.zeros_like(own[:, :, 0])
        arrived = []
        for step in range(steps):
            send = jnp.where(is_owner, own[:, :, min(step, chunks - 1)], held)
            held = lax.ppermute(send, "row", pairs)
            arrived.append(held)
        stacked = jnp.stack(arrived, axis=2)
        picked = []
        for p in range(value.shape[0]):
            start = jnp.maximum(distance[p] - 1, 0)
            picked.append(lax.dynamic_slice_in_dim(stacked[p], start, chunks, 1))
        picked = jnp.where(is_owner[..., None], own, jnp.stack(picked))
        halves.append(picked.reshape(*picked.shape[:2], -1, *picked.shape[4:]))
    return jnp.concatenate(halves, axis=2)


def to_bf16(value):
    return lax.reduce_precision(value, exponent_bits=8, mantissa_bits=7).astype(jnp.bfloat16)


def body(traces, prior, bins, panels):
    sample_count, shots_local, receivers = traces.shape
    row_count = lax.axis_size("row")
    freq_count = lax.axis_size("freq")
    block_rows = receivers // row_count
    sample_index = BLOCK_START + jnp.arange(sample_count, dtype=jnp.int32)
    turn_count = bins[:, None] * sample_index[None, :] % NT_REC
    angles = 2.0 * math.pi / NT_REC * turn_count.astype(jnp.float32)
    twiddle = jnp.stack([jnp.cos(angles), -jnp.sin(angles)], axis=1).astype(jnp.bfloat16)
    own_twiddle = lax.dynamic_index_in_dim(twiddle, lax.axis_index("freq"), 0, keepdims=False)
    weights = own_twiddle.astype(jnp.float32)
    piece = shots_local // PIECES
    groups = freq_count * row_count
    prior_blocks = prior[0].reshape(2, groups, PIECES, piece, block_rows)
    panels_each = block_rows // PANEL
    offsets = [panels[p] % panels_each * PANEL for p in range(STEPS)]

    def transform(samples):
        total = weights[:, 0, None, None] * samples[0] + weights[:, 1, None, None] * samples[1]
        return lax.reduce_precision(total, exponent_bits=8, mantissa_bits=7)

    parts = []
    panel_samples = [[] for _ in range(STEPS)]
    for index in range(PIECES):
        chunk = traces[:, index * piece:(index + 1) * piece, :]
        by_row = lax.all_to_all(chunk, "row", split_axis=2, concat_axis=1, tiled=True)
        gathered = lax.all_gather(by_row, "freq", axis=1, tiled=True)
        for p in range(STEPS):
            picked = lax.dynamic_slice_in_dim(gathered, offsets[p], PANEL, 2)
            panel_samples[p].append(picked.reshape(sample_count, groups, piece, PANEL))
        samples = gathered.astype(jnp.float32).reshape(sample_count, groups * piece, block_rows)
        blocks = prior_blocks[:, :, index].reshape(2, groups * piece, block_rows)
        parts.append(to_bf16(blocks.astype(jnp.float32) + transform(samples)).reshape(2, groups, piece, block_rows))
    spectrum = jnp.stack(parts, axis=2).reshape(2, receivers, block_rows)
    own_panels = []
    for p in range(STEPS):
        samples = jnp.stack(panel_samples[p], axis=2).reshape(sample_count, receivers, PANEL).astype(jnp.float32)
        prior_rows = lax.dynamic_slice_in_dim(prior[0], offsets[p], PANEL, 2).astype(jnp.float32)
        own_panels.append(to_bf16(prior_rows + transform(samples)))
    owners = jnp.stack([panels[p] // panels_each for p in range(STEPS)])
    rights = broadcast(jnp.stack(own_panels), owners, RING_CHUNKS)
    lefts = []
    for p in range(STEPS):
        left = lax.dynamic_slice_in_dim(spectrum, panels[p] * PANEL, PANEL, 1)
        lefts += [left[0], left[1]]
    reals = []
    imags = []
    for right in rights:
        reals += [right[0], -right[1]]
        imags += [right[1], right[0]]
    left_all = jnp.concatenate(lefts, axis=0)
    dims = (((0,), (1,)), ((), ()))
    real_sum = lax.dot_general(left_all, jnp.concatenate(reals, axis=1), dims, preferred_element_type=jnp.float32)
    imag_sum = lax.dot_general(left_all, jnp.concatenate(imags, axis=1), dims, preferred_element_type=jnp.float32)
    return (jnp.stack([real_sum, imag_sum])[None].astype(jnp.bfloat16), spectrum[None])


def solution(mesh):
    return jax.shard_map(
        body,
        mesh=mesh,
        in_specs=(P(None, ("freq", "row"), None), P("freq", None, None, "row"), P(), P()),
        out_specs=(P("freq", None, "row", None), P("freq", None, None, "row")),
        check_vma=False,
    )
```

```python
import math

import jax
import jax.numpy as jnp
from jax import lax
from jax.sharding import PartitionSpec as P

NT_REC = 1024
PANEL = 256
STEPS = 2
BLOCK_START = 1022
PIECES = 4
RING_CHUNKS = 8


def ring_order(count):
    evens = list(range(0, count, 2))
    odds = list(range(1, count, 2))[::-1]
    return evens + odds


def broadcast(value, owners, chunks):
    count = lax.axis_size("row")
    order = ring_order(count)
    place = [0] * count
    for position, member in enumerate(order):
        place[member] = position
    place_of = jnp.array(place, jnp.int32)
    mine = place_of[lax.axis_index("row")]
    owner_place = place_of[owners]
    forward = [(order[i], order[(i + 1) % count]) for i in range(count)]
    backward = [(order[(i + 1) % count], order[i]) for i in range(count)]
    steps = chunks + count - 2
    lead = (1,) * (value.ndim - 1)
    halves = []
    for direction, pairs in ((0, forward), (1, backward)):
        if direction == 0:
            distance = (mine - owner_place) % count
        else:
            distance = (owner_place - mine) % count
        half = value.shape[2] // 2
        part = value[:, :, direction * half:(direction + 1) * half]
        own = part.reshape(*part.shape[:2], chunks, half // chunks, *part.shape[3:])
        is_owner = (distance == 0).reshape(-1, *lead)
        held = jnp.zeros_like(own[:, :, 0])
        arrived = []
        for step in range(steps):
            send = jnp.where(is_owner, own[:, :, min(step, chunks - 1)], held)
            held = lax.ppermute(send, "row", pairs)
            arrived.append(held)
        stacked = jnp.stack(arrived, axis=2)
        picked = []
        for p in range(value.shape[0]):
            start = jnp.maximum(distance[p] - 1, 0)
            picked.append(lax.dynamic_slice_in_dim(stacked[p], start, chunks, 1))
        picked = jnp.where(is_owner[..., None], own, jnp.stack(picked))
        halves.append(picked.reshape(*picked.shape[:2], -1, *picked.shape[4:]))
    return jnp.concatenate(halves, axis=2)


def to_bf16(value):
    return lax.reduce_precision(value, exponent_bits=8, mantissa_bits=7).astype(jnp.bfloat16)


def body(traces, prior, bins, panels):
    sample_count, shots_local, receivers = traces.shape
    row_count = lax.axis_size("row")
    freq_count = lax.axis_size("freq")
    block_rows = receivers // row_count
    sample_index = BLOCK_START + jnp.arange(sample_count, dtype=jnp.int32)
    turn_count = bins[:, None] * sample_index[None, :] % NT_REC
    angles = 2.0 * math.pi / NT_REC * turn_count.astype(jnp.float32)
    twiddle = jnp.stack([jnp.cos(angles), -jnp.sin(angles)], axis=1).astype(jnp.bfloat16)
    own_twiddle = lax.dynamic_index_in_dim(twiddle, lax.axis_index("freq"), 0, keepdims=False)
    weights = own_twiddle.astype(jnp.float32)
    piece = shots_local // PIECES
    groups = freq_count * row_count
    prior_blocks = prior[0].reshape(2, groups, PIECES, piece, block_rows)
    samples = []
    for index in range(PIECES):
        chunk = traces[:, index * piece:(index + 1) * piece, :]
        by_row = lax.all_to_all(chunk, "row", split_axis=2, concat_axis=1, tiled=True)
        gathered = lax.all_gather(by_row, "freq", axis=1, tiled=True)
        samples.append(gathered.reshape(sample_count, groups, piece, block_rows))
    samples = jnp.stack(samples, axis=2).reshape(sample_count, receivers, block_rows).astype(jnp.float32)
    transformed = weights[:, 0, None, None] * samples[0] + weights[:, 1, None, None] * samples[1]
    transformed = lax.reduce_precision(transformed, exponent_bits=8, mantissa_bits=7)
    spectrum = to_bf16(prior[0].astype(jnp.float32) + transformed)
    panels_each = block_rows // PANEL
    own_panels = []
    lefts = []
    for panel_step in range(STEPS):
        chosen = panels[panel_step]
        offset = chosen % panels_each * PANEL
        own_panels.append(lax.dynamic_slice_in_dim(spectrum, offset, PANEL, 2))
        left = lax.dynamic_slice_in_dim(spectrum, chosen * PANEL, PANEL, 1)
        lefts += [left[0], left[1]]
    owners = jnp.stack([panels[p] // panels_each for p in range(STEPS)])
    rights = broadcast(jnp.stack(own_panels), owners, RING_CHUNKS)
    reals = []
    imags = []
    for right in rights:
        reals += [right[0], -right[1]]
        imags += [right[1], right[0]]
    left_all = jnp.concatenate(lefts, axis=0)
    left_pair = jnp.stack([left_all, left_all])
    right_pair = jnp.stack([jnp.concatenate(reals, axis=1), jnp.concatenate(imags, axis=1)])
    dims = (((1,), (2,)), ((0,), (0,)))
    sums = lax.dot_general(left_pair, right_pair, dims, preferred_element_type=jnp.float32)
    return (sums[None].astype(jnp.bfloat16), spectrum[None])


def solution(mesh):
    return jax.shard_map(
        body,
        mesh=mesh,
        in_specs=(P(None, ("freq", "row"), None), P("freq", None, None, "row"), P(), P()),
        out_specs=(P("freq", None, "row", None), P("freq", None, None, "row")),
        check_vma=False,
    )
```

```python
import math

import jax
import jax.numpy as jnp
from jax import lax
from jax.sharding import PartitionSpec as P

NT_REC = 1024
PANEL = 256
STEPS = 2
BLOCK_START = 1022
PIECES = 2
RING_CHUNKS = 8


def ring_order(count):
    evens = list(range(0, count, 2))
    odds = list(range(1, count, 2))[::-1]
    return evens + odds


def broadcast(value, owners, chunks):
    count = lax.axis_size("row")
    order = ring_order(count)
    place = [0] * count
    for position, member in enumerate(order):
        place[member] = position
    place_of = jnp.array(place, jnp.int32)
    mine = place_of[lax.axis_index("row")]
    owner_place = place_of[owners]
    forward = [(order[i], order[(i + 1) % count]) for i in range(count)]
    backward = [(order[(i + 1) % count], order[i]) for i in range(count)]
    steps = chunks + count - 2
    lead = (1,) * (value.ndim - 1)
    halves = []
    for direction, pairs in ((0, forward), (1, backward)):
        if direction == 0:
            distance = (mine - owner_place) % count
        else:
            distance = (owner_place - mine) % count
        half = value.shape[2] // 2
        part = value[:, :, direction * half:(direction + 1) * half]
        own = part.reshape(*part.shape[:2], chunks, half // chunks, *part.shape[3:])
        is_owner = (distance == 0).reshape(-1, *lead)
        held = jnp.zeros_like(own[:, :, 0])
        arrived = []
        for step in range(steps):
            send = jnp.where(is_owner, own[:, :, min(step, chunks - 1)], held)
            held = lax.ppermute(send, "row", pairs)
            arrived.append(held)
        stacked = jnp.stack(arrived, axis=2)
        picked = []
        for p in range(value.shape[0]):
            start = jnp.maximum(distance[p] - 1, 0)
            picked.append(lax.dynamic_slice_in_dim(stacked[p], start, chunks, 1))
        picked = jnp.where(is_owner[..., None], own, jnp.stack(picked))
        halves.append(picked.reshape(*picked.shape[:2], -1, *picked.shape[4:]))
    return jnp.concatenate(halves, axis=2)


def to_bf16(value):
    return lax.reduce_precision(value, exponent_bits=8, mantissa_bits=7).astype(jnp.bfloat16)


def body(traces, prior, bins, panels):
    sample_count, shots_local, receivers = traces.shape
    row_count = lax.axis_size("row")
    freq_count = lax.axis_size("freq")
    block_rows = receivers // row_count
    sample_index = BLOCK_START + jnp.arange(sample_count, dtype=jnp.int32)
    turn_count = bins[:, None] * sample_index[None, :] % NT_REC
    angles = 2.0 * math.pi / NT_REC * turn_count.astype(jnp.float32)
    twiddle = jnp.stack([jnp.cos(angles), -jnp.sin(angles)], axis=1).astype(jnp.bfloat16)
    own_twiddle = lax.dynamic_index_in_dim(twiddle, lax.axis_index("freq"), 0, keepdims=False)
    weights = own_twiddle.astype(jnp.float32)
    piece = shots_local // PIECES
    groups = freq_count * row_count
    prior_blocks = prior[0].reshape(2, groups, PIECES, piece, block_rows)
    parts = []
    for index in range(PIECES):
        chunk = traces[:, index * piece:(index + 1) * piece, :]
        by_row = lax.all_to_all(chunk, "row", split_axis=2, concat_axis=1, tiled=True)
        gathered = lax.all_gather(by_row, "freq", axis=1, tiled=True)
        gathered = gathered.reshape(sample_count, groups, piece, block_rows)
        first = gathered[0].astype(jnp.float32)
        second = gathered[1].astype(jnp.float32)
        transformed = weights[:, 0, None, None, None] * first + weights[:, 1, None, None, None] * second
        transformed = lax.reduce_precision(transformed, exponent_bits=8, mantissa_bits=7)
        parts.append(to_bf16(prior_blocks[:, :, index].astype(jnp.float32) + transformed))
    spectrum = jnp.stack(parts, axis=2).reshape(2, receivers, block_rows)
    panels_each = block_rows // PANEL
    own_panels = []
    lefts = []
    for panel_step in range(STEPS):
        chosen = panels[panel_step]
        offset = chosen % panels_each * PANEL
        own_panels.append(lax.dynamic_slice_in_dim(spectrum, offset, PANEL, 2))
        left = lax.dynamic_slice_in_dim(spectrum, chosen * PANEL, PANEL, 1)
        lefts += [left[0], left[1]]
    owners = jnp.stack([panels[p] // panels_each for p in range(STEPS)])
    rights = broadcast(jnp.stack(own_panels), owners, RING_CHUNKS)
    reals = []
    imags = []
    for right in rights:
        reals += [right[0], -right[1]]
        imags += [right[1], right[0]]
    left_all = jnp.concatenate(lefts, axis=0)
    dims = (((0,), (1,)), ((), ()))
    real_sum = lax.dot_general(left_all, jnp.concatenate(reals, axis=1), dims, preferred_element_type=jnp.float32)
    imag_sum = lax.dot_general(left_all, jnp.concatenate(imags, axis=1), dims, preferred_element_type=jnp.float32)
    return (jnp.stack([real_sum, imag_sum])[None].astype(jnp.bfloat16), spectrum[None])


def solution(mesh):
    return jax.shard_map(
        body,
        mesh=mesh,
        in_specs=(P(None, ("freq", "row"), None), P("freq", None, None, "row"), P(), P()),
        out_specs=(P("freq", None, "row", None), P("freq", None, None, "row")),
        check_vma=False,
    )
```

```python
import math

import jax
import jax.numpy as jnp
from jax import lax
from jax.experimental import pallas as pl
from jax.experimental.pallas import tpu as pltpu
from jax.sharding import PartitionSpec as P

NT_REC = 1024
PANEL = 256
STEPS = 2
BLOCK_START = 1022
PIECES = 2
RING_CHUNKS = 8


def ring_order(count):
    evens = list(range(0, count, 2))
    odds = list(range(1, count, 2))[::-1]
    return evens + odds


def broadcast(values, owners, chunks):
    count = lax.axis_size("row")
    order = ring_order(count)
    place = [0] * count
    for position, member in enumerate(order):
        place[member] = position
    place_of = jnp.array(place, jnp.int32)
    mine = place_of[lax.axis_index("row")]
    forward = [(order[i], order[(i + 1) % count]) for i in range(count)]
    backward = [(order[(i + 1) % count], order[i]) for i in range(count)]
    steps = chunks + count - 2
    halves = []
    for direction, pairs in ((0, forward), (1, backward)):
        distance = []
        own = []
        for value, owner in zip(values, owners):
            if direction == 0:
                distance.append((mine - place_of[owner]) % count)
            else:
                distance.append((place_of[owner] - mine) % count)
            half = value.shape[1] // 2
            part = value[:, direction * half:(direction + 1) * half]
            own.append(part.reshape(part.shape[0], chunks, half // chunks, *part.shape[2:]))
        held = [jnp.zeros_like(piece[:, 0]) for piece in own]
        arrived = [[] for _ in values]
        for step in range(steps):
            send = [
                jnp.where(distance[p] == 0, own[p][:, min(step, chunks - 1)], held[p])
                for p in range(len(values))
            ]
            held = lax.ppermute(send, "row", pairs)
            for p in range(len(values)):
                arrived[p].append(held[p])
        results = []
        for p in range(len(values)):
            stacked = jnp.stack(arrived[p], axis=1)
            start = jnp.maximum(distance[p] - 1, 0)
            picked = lax.dynamic_slice_in_dim(stacked, start, chunks, 1)
            picked = jnp.where(distance[p] == 0, own[p], picked)
            results.append(picked.reshape(picked.shape[0], -1, *picked.shape[3:]))
        halves.append(results)
    return [jnp.concatenate([halves[0][p], halves[1][p]], axis=1) for p in range(len(values))]


def spectrum_kernel(weight_ref, first_ref, second_ref, prior_ref, out_ref):
    piece = first_ref.shape[1]
    for half, source_ref in enumerate((first_ref, second_ref)):
        early = source_ref[0].astype(jnp.float32)
        late = source_ref[1].astype(jnp.float32)
        rows = pl.ds(half * piece, piece)
        for part in range(2):
            total = weight_ref[2 * part] * early + weight_ref[2 * part + 1] * late
            total = total.astype(jnp.bfloat16).astype(jnp.float32)
            out_ref[part, rows, :] = (prior_ref[part, rows, :].astype(jnp.float32) + total).astype(jnp.bfloat16)


def make_spectrum(weights, first, second, prior_block, piece):
    parts, shots, columns = prior_block.shape
    groups = first.shape[1] // piece
    half_spec = pl.BlockSpec((parts, piece, columns), lambda g: (0, g, 0))
    whole_spec = pl.BlockSpec((parts, 2 * piece, columns), lambda g: (0, g, 0))
    return pl.pallas_call(
        spectrum_kernel,
        grid=(groups,),
        in_specs=[pl.BlockSpec(memory_space=pltpu.SMEM), half_spec, half_spec, whole_spec],
        out_specs=whole_spec,
        out_shape=jax.ShapeDtypeStruct(prior_block.shape, jnp.bfloat16),
        cost_estimate=pl.CostEstimate(
            flops=8 * parts * shots * columns, transcendentals=0, bytes_accessed=6 * parts * shots * columns
        ),
    )(weights.reshape(-1), first, second, prior_block)


def to_bf16(value):
    return lax.reduce_precision(value, exponent_bits=8, mantissa_bits=7).astype(jnp.bfloat16)


def body(traces, prior, bins, panels):
    sample_count, shots_local, receivers = traces.shape
    row_count = lax.axis_size("row")
    block_rows = receivers // row_count
    sample_index = BLOCK_START + jnp.arange(sample_count, dtype=jnp.int32)
    turn_count = bins[:, None] * sample_index[None, :] % NT_REC
    angles = 2.0 * math.pi / NT_REC * turn_count.astype(jnp.float32)
    twiddle = jnp.stack([jnp.cos(angles), -jnp.sin(angles)], axis=1).astype(jnp.bfloat16)
    own_twiddle = lax.dynamic_index_in_dim(twiddle, lax.axis_index("freq"), 0, keepdims=False)
    weights = own_twiddle.astype(jnp.float32)
    piece = shots_local // PIECES
    halves = []
    for index in range(PIECES):
        chunk = traces[:, index * piece:(index + 1) * piece, :]
        by_row = lax.all_to_all(chunk, "row", split_axis=2, concat_axis=1, tiled=True)
        halves.append(lax.all_gather(by_row, "freq", axis=1, tiled=True))
    spectrum = make_spectrum(weights, halves[0], halves[1], prior[0], piece)
    panels_each = block_rows // PANEL
    lefts = []
    rights = []
    for panel_step in range(STEPS):
        chosen = panels[panel_step]
        offset = chosen % panels_each * PANEL
        own_rows = lax.dynamic_slice_in_dim(spectrum, offset, PANEL, 2)
        rights.append(own_rows)
        lefts.append(lax.dynamic_slice_in_dim(spectrum, chosen * PANEL, PANEL, 1))
    owners = [panels[p] // panels_each for p in range(STEPS)]
    rights = broadcast(rights, owners, RING_CHUNKS)
    real_left = []
    imag_left = []
    shared = []
    for left, right in zip(lefts, rights):
        real_left += [left[0], -left[1]]
        imag_left += [left[1], left[0]]
        shared += [right[0], right[1]]
    left_pair = jnp.stack([jnp.concatenate(real_left, axis=0), jnp.concatenate(imag_left, axis=0)])
    dims = (((1,), (1,)), ((), ()))
    sums = lax.dot_general(left_pair, jnp.concatenate(shared, axis=1), dims, preferred_element_type=jnp.float32)
    return (sums[None].astype(jnp.bfloat16), spectrum[None])


def solution(mesh):
    return jax.shard_map(
        body,
        mesh=mesh,
        in_specs=(P(None, ("freq", "row"), None), P("freq", None, None, "row"), P(), P()),
        out_specs=(P("freq", None, "row", None), P("freq", None, None, "row")),
        check_vma=False,
    )
```

```python
import math

import jax
import jax.numpy as jnp
from jax import lax
from jax.experimental import pallas as pl
from jax.experimental.pallas import tpu as pltpu
from jax.sharding import PartitionSpec as P

NT_REC = 1024
PANEL = 256
STEPS = 2
BLOCK_START = 1022
PIECES = 2
RING_CHUNKS = 8


def ring_order(count):
    evens = list(range(0, count, 2))
    odds = list(range(1, count, 2))[::-1]
    return evens + odds


def broadcast(values, owners, chunks):
    count = lax.axis_size("row")
    order = ring_order(count)
    place = [0] * count
    for position, member in enumerate(order):
        place[member] = position
    place_of = jnp.array(place, jnp.int32)
    mine = place_of[lax.axis_index("row")]
    forward = [(order[i], order[(i + 1) % count]) for i in range(count)]
    backward = [(order[(i + 1) % count], order[i]) for i in range(count)]
    steps = chunks + count - 2
    halves = []
    for direction, pairs in ((0, forward), (1, backward)):
        distance = []
        own = []
        for value, owner in zip(values, owners):
            if direction == 0:
                distance.append((mine - place_of[owner]) % count)
            else:
                distance.append((place_of[owner] - mine) % count)
            half = value.shape[1] // 2
            part = value[:, direction * half:(direction + 1) * half]
            own.append(part.reshape(part.shape[0], chunks, half // chunks, *part.shape[2:]))
        held = [jnp.zeros_like(piece[:, 0]) for piece in own]
        arrived = [[] for _ in values]
        for step in range(steps):
            send = [
                jnp.where(distance[p] == 0, own[p][:, min(step, chunks - 1)], held[p])
                for p in range(len(values))
            ]
            held = lax.ppermute(send, "row", pairs)
            for p in range(len(values)):
                arrived[p].append(held[p])
        results = []
        for p in range(len(values)):
            stacked = jnp.stack(arrived[p], axis=1)
            start = jnp.maximum(distance[p] - 1, 0)
            picked = lax.dynamic_slice_in_dim(stacked, start, chunks, 1)
            picked = jnp.where(distance[p] == 0, own[p], picked)
            results.append(picked.reshape(picked.shape[0], -1, *picked.shape[3:]))
        halves.append(results)
    return [jnp.concatenate([halves[0][p], halves[1][p]], axis=1) for p in range(len(values))]


def spectrum_kernel(weight_ref, source_ref, prior_ref, *rest):
    out_ref = rest[-1]
    early = source_ref[0].astype(jnp.float32)
    late = source_ref[1].astype(jnp.float32)
    for part in range(2):
        total = weight_ref[2 * part] * early + weight_ref[2 * part + 1] * late
        total = total.astype(jnp.bfloat16).astype(jnp.float32)
        out_ref[part] = (prior_ref[part].astype(jnp.float32) + total).astype(jnp.bfloat16)


def make_spectrum(weights, first, second, prior_block, piece):
    parts, shots, columns = prior_block.shape
    groups = first.shape[1] // piece
    half_spec = pl.BlockSpec((parts, piece, columns), lambda g: (0, g, 0))
    cost = pl.CostEstimate(flops=4 * parts * shots * columns, transcendentals=0, bytes_accessed=3 * parts * shots * columns)
    result = None
    for half, source in enumerate((first, second)):
        place_spec = pl.BlockSpec((parts, piece, columns), lambda g, half=half: (0, 2 * g + half, 0))
        operands = [weights.reshape(-1), source, prior_block]
        in_specs = [pl.BlockSpec(memory_space=pltpu.SMEM), half_spec, place_spec]
        aliases = {}
        if result is not None:
            operands.append(result)
            in_specs.append(pl.BlockSpec(memory_space=pl.ANY))
            aliases = {3: 0}
        result = pl.pallas_call(
            spectrum_kernel,
            grid=(groups,),
            in_specs=in_specs,
            out_specs=place_spec,
            out_shape=jax.ShapeDtypeStruct(prior_block.shape, jnp.bfloat16),
            input_output_aliases=aliases,
            cost_estimate=cost,
        )(*operands)
    return result


def to_bf16(value):
    return lax.reduce_precision(value, exponent_bits=8, mantissa_bits=7).astype(jnp.bfloat16)


def body(traces, prior, bins, panels):
    sample_count, shots_local, receivers = traces.shape
    row_count = lax.axis_size("row")
    block_rows = receivers // row_count
    sample_index = BLOCK_START + jnp.arange(sample_count, dtype=jnp.int32)
    turn_count = bins[:, None] * sample_index[None, :] % NT_REC
    angles = 2.0 * math.pi / NT_REC * turn_count.astype(jnp.float32)
    twiddle = jnp.stack([jnp.cos(angles), -jnp.sin(angles)], axis=1).astype(jnp.bfloat16)
    own_twiddle = lax.dynamic_index_in_dim(twiddle, lax.axis_index("freq"), 0, keepdims=False)
    weights = own_twiddle.astype(jnp.float32)
    piece = shots_local // PIECES
    halves = []
    for index in range(PIECES):
        chunk = traces[:, index * piece:(index + 1) * piece, :]
        by_row = lax.all_to_all(chunk, "row", split_axis=2, concat_axis=1, tiled=True)
        halves.append(lax.all_gather(by_row, "freq", axis=1, tiled=True))
    spectrum = make_spectrum(weights, halves[0], halves[1], prior[0], piece)
    panels_each = block_rows // PANEL
    lefts = []
    rights = []
    for panel_step in range(STEPS):
        chosen = panels[panel_step]
        offset = chosen % panels_each * PANEL
        own_rows = lax.dynamic_slice_in_dim(spectrum, offset, PANEL, 2)
        rights.append(own_rows)
        lefts.append(lax.dynamic_slice_in_dim(spectrum, chosen * PANEL, PANEL, 1))
    owners = [panels[p] // panels_each for p in range(STEPS)]
    rights = broadcast(rights, owners, RING_CHUNKS)
    real_left = []
    imag_left = []
    shared = []
    for left, right in zip(lefts, rights):
        real_left += [left[0], -left[1]]
        imag_left += [left[1], left[0]]
        shared += [right[0], right[1]]
    left_pair = jnp.stack([jnp.concatenate(real_left, axis=0), jnp.concatenate(imag_left, axis=0)])
    dims = (((1,), (1,)), ((), ()))
    sums = lax.dot_general(left_pair, jnp.concatenate(shared, axis=1), dims, preferred_element_type=jnp.float32)
    return (sums[None].astype(jnp.bfloat16), spectrum[None])


def solution(mesh):
    return jax.shard_map(
        body,
        mesh=mesh,
        in_specs=(P(None, ("freq", "row"), None), P("freq", None, None, "row"), P(), P()),
        out_specs=(P("freq", None, "row", None), P("freq", None, None, "row")),
        check_vma=False,
    )
```

```python
import math

import jax
import jax.numpy as jnp
from jax import lax
from jax.experimental import pallas as pl
from jax.experimental.pallas import tpu as pltpu
from jax.sharding import PartitionSpec as P

NT_REC = 1024
PANEL = 256
STEPS = 2
BLOCK_START = 1022
PIECES = 2
RING_CHUNKS = 8


def ring_order(count):
    evens = list(range(0, count, 2))
    odds = list(range(1, count, 2))[::-1]
    return evens + odds


def broadcast(values, owners, chunks):
    count = lax.axis_size("row")
    order = ring_order(count)
    place = [0] * count
    for position, member in enumerate(order):
        place[member] = position
    place_of = jnp.array(place, jnp.int32)
    mine = place_of[lax.axis_index("row")]
    forward = [(order[i], order[(i + 1) % count]) for i in range(count)]
    backward = [(order[(i + 1) % count], order[i]) for i in range(count)]
    steps = chunks + count - 2
    halves = []
    for direction, pairs in ((0, forward), (1, backward)):
        distance = []
        own = []
        for value, owner in zip(values, owners):
            if direction == 0:
                distance.append((mine - place_of[owner]) % count)
            else:
                distance.append((place_of[owner] - mine) % count)
            half = value.shape[1] // 2
            part = value[:, direction * half:(direction + 1) * half]
            own.append(part.reshape(part.shape[0], chunks, half // chunks, *part.shape[2:]))
        held = [jnp.zeros_like(piece[:, 0]) for piece in own]
        arrived = [[] for _ in values]
        for step in range(steps):
            if step < chunks:
                send = [jnp.where(distance[p] == 0, own[p][:, step], held[p]) for p in range(len(values))]
            else:
                send = held
            held = lax.ppermute(send, "row", pairs)
            for p in range(len(values)):
                arrived[p].append(held[p])
        results = []
        for p in range(len(values)):
            stacked = jnp.stack(arrived[p], axis=1)
            start = jnp.maximum(distance[p] - 1, 0)
            picked = lax.dynamic_slice_in_dim(stacked, start, chunks, 1)
            picked = jnp.where(distance[p] == 0, own[p], picked)
            results.append(picked.reshape(picked.shape[0], -1, *picked.shape[3:]))
        halves.append(results)
    return [jnp.concatenate([halves[0][p], halves[1][p]], axis=1) for p in range(len(values))]


def spectrum_kernel(weight_ref, source_ref, prior_ref, *rest):
    out_ref = rest[-1]
    early = source_ref[0].astype(jnp.float32)
    late = source_ref[1].astype(jnp.float32)
    for part in range(2):
        total = weight_ref[2 * part] * early + weight_ref[2 * part + 1] * late
        total = total.astype(jnp.bfloat16).astype(jnp.float32)
        out_ref[part] = (prior_ref[part].astype(jnp.float32) + total).astype(jnp.bfloat16)


def make_spectrum(weights, first, second, prior_block, piece):
    parts, shots, columns = prior_block.shape
    groups = first.shape[1] // piece
    half_spec = pl.BlockSpec((parts, piece, columns), lambda g: (0, g, 0))
    cost = pl.CostEstimate(flops=4 * parts * shots * columns, transcendentals=0, bytes_accessed=3 * parts * shots * columns)
    result = None
    for half, source in enumerate((first, second)):
        place_spec = pl.BlockSpec((parts, piece, columns), lambda g, half=half: (0, 2 * g + half, 0))
        operands = [weights.reshape(-1), source, prior_block]
        in_specs = [pl.BlockSpec(memory_space=pltpu.SMEM), half_spec, place_spec]
        aliases = {}
        if result is not None:
            operands.append(result)
            in_specs.append(pl.BlockSpec(memory_space=pl.ANY))
            aliases = {3: 0}
        result = pl.pallas_call(
            spectrum_kernel,
            grid=(groups,),
            in_specs=in_specs,
            out_specs=place_spec,
            out_shape=jax.ShapeDtypeStruct(prior_block.shape, jnp.bfloat16),
            input_output_aliases=aliases,
            cost_estimate=cost,
        )(*operands)
    return result


def to_bf16(value):
    return lax.reduce_precision(value, exponent_bits=8, mantissa_bits=7).astype(jnp.bfloat16)


def body(traces, prior, bins, panels):
    sample_count, shots_local, receivers = traces.shape
    row_count = lax.axis_size("row")
    block_rows = receivers // row_count
    sample_index = BLOCK_START + jnp.arange(sample_count, dtype=jnp.int32)
    turn_count = bins[:, None] * sample_index[None, :] % NT_REC
    angles = 2.0 * math.pi / NT_REC * turn_count.astype(jnp.float32)
    twiddle = jnp.stack([jnp.cos(angles), -jnp.sin(angles)], axis=1).astype(jnp.bfloat16)
    own_twiddle = lax.dynamic_index_in_dim(twiddle, lax.axis_index("freq"), 0, keepdims=False)
    weights = own_twiddle.astype(jnp.float32)
    piece = shots_local // PIECES
    halves = []
    for index in range(PIECES):
        chunk = traces[:, index * piece:(index + 1) * piece, :]
        by_row = lax.all_to_all(chunk, "row", split_axis=2, concat_axis=1, tiled=True)
        halves.append(lax.all_gather(by_row, "freq", axis=1, tiled=True))
    spectrum = make_spectrum(weights, halves[0], halves[1], prior[0], piece)
    panels_each = block_rows // PANEL
    lefts = []
    rights = []
    for panel_step in range(STEPS):
        chosen = panels[panel_step]
        offset = chosen % panels_each * PANEL
        own_rows = lax.dynamic_slice_in_dim(spectrum, offset, PANEL, 2)
        rights.append(own_rows)
        lefts.append(lax.dynamic_slice_in_dim(spectrum, chosen * PANEL, PANEL, 1))
    owners = [panels[p] // panels_each for p in range(STEPS)]
    rights = broadcast(rights, owners, RING_CHUNKS)
    real_left = []
    imag_left = []
    shared = []
    for left, right in zip(lefts, rights):
        real_left += [left[0], -left[1]]
        imag_left += [left[1], left[0]]
        shared += [right[0], right[1]]
    left_pair = jnp.stack([jnp.concatenate(real_left, axis=0), jnp.concatenate(imag_left, axis=0)])
    dims = (((1,), (1,)), ((), ()))
    sums = lax.dot_general(left_pair, jnp.concatenate(shared, axis=1), dims, preferred_element_type=jnp.float32)
    return (sums[None].astype(jnp.bfloat16), spectrum[None])


def solution(mesh):
    return jax.shard_map(
        body,
        mesh=mesh,
        in_specs=(P(None, ("freq", "row"), None), P("freq", None, None, "row"), P(), P()),
        out_specs=(P("freq", None, "row", None), P("freq", None, None, "row")),
        check_vma=False,
    )
```

```python
import math

import jax
import jax.numpy as jnp
from jax import lax
from jax.experimental import pallas as pl
from jax.experimental.pallas import tpu as pltpu
from jax.sharding import PartitionSpec as P

NT_REC = 1024
PANEL = 256
STEPS = 2
BLOCK_START = 1022
PIECES = 2
RING_CHUNKS = 16


def ring_order(count):
    evens = list(range(0, count, 2))
    odds = list(range(1, count, 2))[::-1]
    return evens + odds


def broadcast(values, owners, chunks):
    count = lax.axis_size("row")
    order = ring_order(count)
    place = [0] * count
    for position, member in enumerate(order):
        place[member] = position
    place_of = jnp.array(place, jnp.int32)
    mine = place_of[lax.axis_index("row")]
    forward = [(order[i], order[(i + 1) % count]) for i in range(count)]
    backward = [(order[(i + 1) % count], order[i]) for i in range(count)]
    steps = chunks + count - 2
    halves = []
    for direction, pairs in ((0, forward), (1, backward)):
        distance = []
        own = []
        for value, owner in zip(values, owners):
            if direction == 0:
                distance.append((mine - place_of[owner]) % count)
            else:
                distance.append((place_of[owner] - mine) % count)
            half = value.shape[1] // 2
            part = value[:, direction * half:(direction + 1) * half]
            own.append(part.reshape(part.shape[0], chunks, half // chunks, *part.shape[2:]))
        held = [jnp.zeros_like(piece[:, 0]) for piece in own]
        arrived = [[] for _ in values]
        for step in range(steps):
            if step < chunks:
                send = [jnp.where(distance[p] == 0, own[p][:, step], held[p]) for p in range(len(values))]
            else:
                send = held
            held = lax.ppermute(send, "row", pairs)
            for p in range(len(values)):
                arrived[p].append(held[p])
        results = []
        for p in range(len(values)):
            stacked = jnp.stack(arrived[p], axis=1)
            start = jnp.maximum(distance[p] - 1, 0)
            picked = lax.dynamic_slice_in_dim(stacked, start, chunks, 1)
            picked = jnp.where(distance[p] == 0, own[p], picked)
            results.append(picked.reshape(picked.shape[0], -1, *picked.shape[3:]))
        halves.append(results)
    return [jnp.concatenate([halves[0][p], halves[1][p]], axis=1) for p in range(len(values))]


def spectrum_kernel(weight_ref, source_ref, prior_ref, *rest):
    out_ref = rest[-1]
    early = source_ref[0].astype(jnp.float32)
    late = source_ref[1].astype(jnp.float32)
    for part in range(2):
        total = weight_ref[2 * part] * early + weight_ref[2 * part + 1] * late
        total = total.astype(jnp.bfloat16).astype(jnp.float32)
        out_ref[part] = (prior_ref[part].astype(jnp.float32) + total).astype(jnp.bfloat16)


def make_spectrum(weights, first, second, prior_block, piece):
    parts, shots, columns = prior_block.shape
    groups = first.shape[1] // piece
    half_spec = pl.BlockSpec((parts, piece, columns), lambda g: (0, g, 0))
    cost = pl.CostEstimate(flops=4 * parts * shots * columns, transcendentals=0, bytes_accessed=3 * parts * shots * columns)
    result = None
    for half, source in enumerate((first, second)):
        place_spec = pl.BlockSpec((parts, piece, columns), lambda g, half=half: (0, 2 * g + half, 0))
        operands = [weights.reshape(-1), source, prior_block]
        in_specs = [pl.BlockSpec(memory_space=pltpu.SMEM), half_spec, place_spec]
        aliases = {}
        if result is not None:
            operands.append(result)
            in_specs.append(pl.BlockSpec(memory_space=pl.ANY))
            aliases = {3: 0}
        result = pl.pallas_call(
            spectrum_kernel,
            grid=(groups,),
            in_specs=in_specs,
            out_specs=place_spec,
            out_shape=jax.ShapeDtypeStruct(prior_block.shape, jnp.bfloat16),
            input_output_aliases=aliases,
            cost_estimate=cost,
        )(*operands)
    return result


def to_bf16(value):
    return lax.reduce_precision(value, exponent_bits=8, mantissa_bits=7).astype(jnp.bfloat16)


def body(traces, prior, bins, panels):
    sample_count, shots_local, receivers = traces.shape
    row_count = lax.axis_size("row")
    block_rows = receivers // row_count
    sample_index = BLOCK_START + jnp.arange(sample_count, dtype=jnp.int32)
    turn_count = bins[:, None] * sample_index[None, :] % NT_REC
    angles = 2.0 * math.pi / NT_REC * turn_count.astype(jnp.float32)
    twiddle = jnp.stack([jnp.cos(angles), -jnp.sin(angles)], axis=1).astype(jnp.bfloat16)
    own_twiddle = lax.dynamic_index_in_dim(twiddle, lax.axis_index("freq"), 0, keepdims=False)
    weights = own_twiddle.astype(jnp.float32)
    piece = shots_local // PIECES
    halves = []
    for index in range(PIECES):
        chunk = traces[:, index * piece:(index + 1) * piece, :]
        by_row = lax.all_to_all(chunk, "row", split_axis=2, concat_axis=1, tiled=True)
        halves.append(lax.all_gather(by_row, "freq", axis=1, tiled=True))
    spectrum = make_spectrum(weights, halves[0], halves[1], prior[0], piece)
    panels_each = block_rows // PANEL
    lefts = []
    rights = []
    for panel_step in range(STEPS):
        chosen = panels[panel_step]
        offset = chosen % panels_each * PANEL
        own_rows = lax.dynamic_slice_in_dim(spectrum, offset, PANEL, 2)
        rights.append(own_rows)
        lefts.append(lax.dynamic_slice_in_dim(spectrum, chosen * PANEL, PANEL, 1))
    owners = [panels[p] // panels_each for p in range(STEPS)]
    rights = broadcast(rights, owners, RING_CHUNKS)
    real_left = []
    imag_left = []
    shared = []
    for left, right in zip(lefts, rights):
        real_left += [left[0], -left[1]]
        imag_left += [left[1], left[0]]
        shared += [right[0], right[1]]
    left_pair = jnp.stack([jnp.concatenate(real_left, axis=0), jnp.concatenate(imag_left, axis=0)])
    dims = (((1,), (1,)), ((), ()))
    sums = lax.dot_general(left_pair, jnp.concatenate(shared, axis=1), dims, preferred_element_type=jnp.float32)
    return (sums[None].astype(jnp.bfloat16), spectrum[None])


def solution(mesh):
    return jax.shard_map(
        body,
        mesh=mesh,
        in_specs=(P(None, ("freq", "row"), None), P("freq", None, None, "row"), P(), P()),
        out_specs=(P("freq", None, "row", None), P("freq", None, None, "row")),
        check_vma=False,
    )
```

```python
import math

import jax
import jax.numpy as jnp
from jax import lax
from jax.experimental import pallas as pl
from jax.experimental.pallas import tpu as pltpu
from jax.sharding import PartitionSpec as P

NT_REC = 1024
PANEL = 256
STEPS = 2
BLOCK_START = 1022
PIECES = 2
RING_CHUNKS = 32


def ring_order(count):
    evens = list(range(0, count, 2))
    odds = list(range(1, count, 2))[::-1]
    return evens + odds


def broadcast(values, owners, chunks):
    count = lax.axis_size("row")
    order = ring_order(count)
    place = [0] * count
    for position, member in enumerate(order):
        place[member] = position
    place_of = jnp.array(place, jnp.int32)
    mine = place_of[lax.axis_index("row")]
    forward = [(order[i], order[(i + 1) % count]) for i in range(count)]
    backward = [(order[(i + 1) % count], order[i]) for i in range(count)]
    steps = chunks + count - 2
    halves = []
    for direction, pairs in ((0, forward), (1, backward)):
        distance = []
        own = []
        for value, owner in zip(values, owners):
            if direction == 0:
                distance.append((mine - place_of[owner]) % count)
            else:
                distance.append((place_of[owner] - mine) % count)
            half = value.shape[1] // 2
            part = value[:, direction * half:(direction + 1) * half]
            own.append(part.reshape(part.shape[0], chunks, half // chunks, *part.shape[2:]))
        held = [jnp.zeros_like(piece[:, 0]) for piece in own]
        arrived = [[] for _ in values]
        for step in range(steps):
            if step < chunks:
                send = [jnp.where(distance[p] == 0, own[p][:, step], held[p]) for p in range(len(values))]
            else:
                send = held
            held = lax.ppermute(send, "row", pairs)
            for p in range(len(values)):
                arrived[p].append(held[p])
        results = []
        for p in range(len(values)):
            stacked = jnp.stack(arrived[p], axis=1)
            start = jnp.maximum(distance[p] - 1, 0)
            picked = lax.dynamic_slice_in_dim(stacked, start, chunks, 1)
            picked = jnp.where(distance[p] == 0, own[p], picked)
            results.append(picked.reshape(picked.shape[0], -1, *picked.shape[3:]))
        halves.append(results)
    return [jnp.concatenate([halves[0][p], halves[1][p]], axis=1) for p in range(len(values))]


def spectrum_kernel(weight_ref, source_ref, prior_ref, *rest):
    out_ref = rest[-1]
    early = source_ref[0].astype(jnp.float32)
    late = source_ref[1].astype(jnp.float32)
    for part in range(2):
        total = weight_ref[2 * part] * early + weight_ref[2 * part + 1] * late
        total = total.astype(jnp.bfloat16).astype(jnp.float32)
        out_ref[part] = (prior_ref[part].astype(jnp.float32) + total).astype(jnp.bfloat16)


def make_spectrum(weights, first, second, prior_block, piece):
    parts, shots, columns = prior_block.shape
    groups = first.shape[1] // piece
    half_spec = pl.BlockSpec((parts, piece, columns), lambda g: (0, g, 0))
    cost = pl.CostEstimate(flops=4 * parts * shots * columns, transcendentals=0, bytes_accessed=3 * parts * shots * columns)
    result = None
    for half, source in enumerate((first, second)):
        place_spec = pl.BlockSpec((parts, piece, columns), lambda g, half=half: (0, 2 * g + half, 0))
        operands = [weights.reshape(-1), source, prior_block]
        in_specs = [pl.BlockSpec(memory_space=pltpu.SMEM), half_spec, place_spec]
        aliases = {}
        if result is not None:
            operands.append(result)
            in_specs.append(pl.BlockSpec(memory_space=pl.ANY))
            aliases = {3: 0}
        result = pl.pallas_call(
            spectrum_kernel,
            grid=(groups,),
            in_specs=in_specs,
            out_specs=place_spec,
            out_shape=jax.ShapeDtypeStruct(prior_block.shape, jnp.bfloat16),
            input_output_aliases=aliases,
            cost_estimate=cost,
        )(*operands)
    return result


def to_bf16(value):
    return lax.reduce_precision(value, exponent_bits=8, mantissa_bits=7).astype(jnp.bfloat16)


def body(traces, prior, bins, panels):
    sample_count, shots_local, receivers = traces.shape
    row_count = lax.axis_size("row")
    block_rows = receivers // row_count
    sample_index = BLOCK_START + jnp.arange(sample_count, dtype=jnp.int32)
    turn_count = bins[:, None] * sample_index[None, :] % NT_REC
    angles = 2.0 * math.pi / NT_REC * turn_count.astype(jnp.float32)
    twiddle = jnp.stack([jnp.cos(angles), -jnp.sin(angles)], axis=1).astype(jnp.bfloat16)
    own_twiddle = lax.dynamic_index_in_dim(twiddle, lax.axis_index("freq"), 0, keepdims=False)
    weights = own_twiddle.astype(jnp.float32)
    piece = shots_local // PIECES
    halves = []
    for index in range(PIECES):
        chunk = traces[:, index * piece:(index + 1) * piece, :]
        by_row = lax.all_to_all(chunk, "row", split_axis=2, concat_axis=1, tiled=True)
        halves.append(lax.all_gather(by_row, "freq", axis=1, tiled=True))
    spectrum = make_spectrum(weights, halves[0], halves[1], prior[0], piece)
    panels_each = block_rows // PANEL
    lefts = []
    rights = []
    for panel_step in range(STEPS):
        chosen = panels[panel_step]
        offset = chosen % panels_each * PANEL
        own_rows = lax.dynamic_slice_in_dim(spectrum, offset, PANEL, 2)
        rights.append(own_rows)
        lefts.append(lax.dynamic_slice_in_dim(spectrum, chosen * PANEL, PANEL, 1))
    owners = [panels[p] // panels_each for p in range(STEPS)]
    rights = broadcast(rights, owners, RING_CHUNKS)
    real_left = []
    imag_left = []
    shared = []
    for left, right in zip(lefts, rights):
        real_left += [left[0], -left[1]]
        imag_left += [left[1], left[0]]
        shared += [right[0], right[1]]
    left_pair = jnp.stack([jnp.concatenate(real_left, axis=0), jnp.concatenate(imag_left, axis=0)])
    dims = (((1,), (1,)), ((), ()))
    sums = lax.dot_general(left_pair, jnp.concatenate(shared, axis=1), dims, preferred_element_type=jnp.float32)
    return (sums[None].astype(jnp.bfloat16), spectrum[None])


def solution(mesh):
    return jax.shard_map(
        body,
        mesh=mesh,
        in_specs=(P(None, ("freq", "row"), None), P("freq", None, None, "row"), P(), P()),
        out_specs=(P("freq", None, "row", None), P("freq", None, None, "row")),
        check_vma=False,
    )
```
